1024 devices in a mesh: space: 128 (over z, x), wave: 8 (over y, core).
Axes of the slice: x: 4, y: 4, z: 32, core: 2. Of those that a mesh axis runs over, the one named last changes fastest.
Arguments:
- wavefunctions: bfloat16 [256, 131072], P('wave', 'space'), may hold values from -48 to 48
- filter_cells: bfloat16 [256, 729, 729], P('space'), may hold values from -1 to 1, as said below
- connectivity: int32 [256, 729], P('space'), may hold values from 0 to 1151, as said below
- owner_list: int32 [16384], P('space'), may hold values from 0 to 1023, as said below
Outputs:
- rotated_block: bfloat16 [256, 131072], P('wave', 'space')
The draws below stay inside these ranges and needn't reach their ends.
Inputs may be any that keep to these rules, and one draw needn't show every extreme that they name: `connectivity`: the cells of each slab form a 2 x 1 x 1 block of cells of degree 8 in a box that is periodic in all three directions, the slabs following one another along the third. Entry l of a cell is the label of its node in that slab (each slab's 1024 labels a permutation of its nodes), or, for a node on the first node plane of the next slab, 1024 plus the node's position in that plane. `owner_list`: entry t * 128 + p is slab t's label of the node at position p of its first node plane. `filter_cells`: each cell's matrix is symmetric.
All inputs are finite; a program needn't handle non-finite values.
Results may differ from the reference program's by a relative error of at most 0.012.
Values may be sent and summed in bfloat16 or wider, within the bound.
No kernel may reach another device: no remote copies, remote signals or barrier semaphores. Data moves between devices by JAX's collectives and lax.ppermute only.
A program may use at most 32 MiB of HBM per device.

```python
import jax
import jax.numpy as jnp
from jax import lax

DEG = 8
NLOC = 729
CX = 2
CY = 1
CZ = 1
SLABS = 128
CELLS_DEV = 2
CELLS = 256
NODES_DEV = 1024
PLANE = 128
NODES = 131072
COLS = 256
DEGREE = 4
NS_ITERS = 4


def node_labels(key):
    base = jax.random.fold_in(key, 9173)
    slab_keys = jax.random.split(base, SLABS)
    labels = jax.vmap(lambda one_key: jax.random.permutation(one_key, NODES_DEV))(slab_keys).astype(jnp.int32)
    chosen_slab = jax.random.randint(jax.random.fold_in(base, 1), (), 0, SLABS)
    first_slot = jax.random.randint(jax.random.fold_in(base, 2), (), 0, PLANE)
    second_slot = (first_slot + 1 + jax.random.randint(jax.random.fold_in(base, 3), (), 0, PLANE - 1)) % PLANE
    chosen_row = labels[chosen_slab]
    held_label = chosen_row[first_slot]
    chosen_row = jnp.where(chosen_row == 0, held_label, jnp.where(chosen_row == held_label, 0, chosen_row))
    held_label = chosen_row[second_slot]
    chosen_row = jnp.where(chosen_row == NODES_DEV - 1, held_label, jnp.where(chosen_row == held_label, NODES_DEV - 1, chosen_row))
    is_chosen = (jnp.arange(SLABS, dtype=jnp.int32) == chosen_slab)[:, None]
    return jnp.where(is_chosen, chosen_row[None, :], labels).astype(jnp.int32)


def draw_connectivity(key, part):
    labels = node_labels(key)
    nodes_x = DEG * CX
    nodes_y = DEG * CY
    local_node = jnp.arange(NLOC, dtype=jnp.int32)
    along_z = local_node // ((DEG + 1) * (DEG + 1))
    along_x = local_node // (DEG + 1) % (DEG + 1)
    along_y = local_node % (DEG + 1)
    cell_number = jnp.arange(CELLS_DEV, dtype=jnp.int32)
    cell_z = cell_number // (CX * CY)
    cell_x = cell_number // CY % CX
    cell_y = cell_number % CY
    node_z = cell_z[:, None] * DEG + along_z[None, :]
    node_x = (cell_x[:, None] * DEG + along_x[None, :]) % nodes_x
    node_y = (cell_y[:, None] * DEG + along_y[None, :]) % nodes_y
    plane_position = node_x * nodes_y + node_y
    structured = jnp.minimum(node_z, DEG * CZ - 1) * (nodes_x * nodes_y) + plane_position
    owned = labels[:, structured]
    result = jnp.where((node_z == DEG * CZ)[None, :, :], NODES_DEV + plane_position[None, :, :], owned)
    return result.reshape(CELLS, NLOC).astype(jnp.int32)


def draw_owner_list(key, part):
    return node_labels(key)[:, :PLANE].reshape(SLABS * PLANE).astype(jnp.int32)


def draw_filter_cells(key, part):
    base = jax.random.fold_in(key, 5521)
    raw_entries = jax.random.normal(base, (CELLS, NLOC, NLOC), jnp.float32)
    symmetric = (raw_entries + jnp.transpose(raw_entries, (0, 2, 1))) * 0.70710678
    log_gains = jax.random.uniform(jax.random.fold_in(base, 1), (CELLS, 1, 1), jnp.float32, jnp.log(0.6), jnp.log(1.3))
    spread = 0.45 / jnp.sqrt(jnp.float32(NLOC))
    return jnp.clip(symmetric * jnp.exp(log_gains) * spread, -1.0, 1.0).astype(jnp.bfloat16)


def draw_wavefunctions(key, part):
    base = jax.random.fold_in(key, 3307)
    noise = jax.random.normal(base, (COLS, NODES), jnp.float32)
    mixing = jnp.eye(COLS, dtype=jnp.float32) + 0.35 * jax.random.normal(jax.random.fold_in(base, 1), (COLS, COLS), jnp.float32) / jnp.sqrt(jnp.float32(COLS))
    centers = jax.random.randint(jax.random.fold_in(base, 2), (COLS,), 0, SLABS)
    slab_number = jnp.arange(SLABS, dtype=jnp.int32)
    distance = jnp.abs(slab_number[None, :] - centers[:, None])
    distance = jnp.minimum(distance, SLABS - distance).astype(jnp.float32)
    envelope = 0.3 + 4.0 * jnp.exp(-0.5 * (distance / 1.5) ** 2)
    mixed = jnp.dot(mixing, noise, precision=jax.lax.Precision.HIGHEST)
    shaped = mixed.reshape(COLS, SLABS, NODES_DEV) * envelope[:, :, None]
    return jnp.clip(shaped.reshape(COLS, NODES), -48.0, 48.0).astype(jnp.bfloat16)


def setup_inputs(seed: int = 0) -> dict:
    arg_keys = jax.random.split(jax.random.key(seed), 5)
    return {
        "wavefunctions": draw_wavefunctions(jax.random.fold_in(arg_keys[4], 71), 0),
        "filter_cells": draw_filter_cells(jax.random.fold_in(arg_keys[4], 71), 0),
        "connectivity": draw_connectivity(jax.random.fold_in(arg_keys[4], 71), 0),
        "owner_list": draw_owner_list(jax.random.fold_in(arg_keys[4], 71), 0),
    }


def global_index(connectivity, owner_list):
    slab_of = jnp.arange(CELLS, dtype=jnp.int32) // CELLS_DEV
    following = (slab_of + 1) % SLABS
    is_remote = connectivity >= NODES_DEV
    plane_slot = jnp.clip(connectivity - NODES_DEV, 0, PLANE - 1)
    remote_label = owner_list[following[:, None] * PLANE + plane_slot]
    own_index = slab_of[:, None] * NODES_DEV + connectivity
    remote_index = following[:, None] * NODES_DEV + remote_label
    return jnp.where(is_remote, remote_index, own_index).astype(jnp.int32)

def apply_filter(wave_block, cell_matrices, node_index):
    rows_block = wave_block.astype(jnp.float32).T

    def one_cell(carried, inputs):
        cell_matrix, indices = inputs
        gathered = jnp.take(rows_block, indices, axis=0)
        product = jnp.dot(cell_matrix.astype(jnp.float32).T, gathered, precision=lax.Precision.HIGHEST, preferred_element_type=jnp.float32)
        return (carried + jax.ops.segment_sum(product, indices, num_segments=NODES), None)
    start_sum = jnp.zeros((NODES, COLS), jnp.float32)
    summed, unused = lax.scan(one_cell, start_sum, (cell_matrices, node_index))
    return summed.T

def newton_schulz(margin):
    highest = lax.Precision.HIGHEST
    scale = jnp.sqrt(jnp.sum(margin * margin) + 1e-06)
    approx = margin / scale
    identity = jnp.eye(COLS, dtype=jnp.float32)
    inverse = identity
    for iteration in range(NS_ITERS):
        middle = 1.5 * identity - 0.5 * jnp.dot(inverse, approx, precision=highest, preferred_element_type=jnp.float32)
        approx = jnp.dot(approx, middle, precision=highest, preferred_element_type=jnp.float32)
        inverse = jnp.dot(middle, inverse, precision=highest, preferred_element_type=jnp.float32)
    return (inverse / jnp.sqrt(scale)).astype(jnp.bfloat16)

def reference(wavefunctions, filter_cells, connectivity, owner_list):
    highest = lax.Precision.HIGHEST
    node_index = global_index(connectivity, owner_list)
    previous = wavefunctions.astype(jnp.float32)
    current = apply_filter(wavefunctions, filter_cells, node_index)
    for degree_step in range(DEGREE - 1):
        following = 2.0 * apply_filter(current.astype(jnp.bfloat16), filter_cells, node_index) - previous
        previous, current = (current, following)
    filtered = current.astype(jnp.bfloat16)
    wide = filtered.astype(jnp.float32)
    margin = jnp.dot(wide, wide.T, precision=highest, preferred_element_type=jnp.float32) / NODES
    rotation = newton_schulz(margin)
    return jnp.dot(rotation.astype(jnp.float32).T, wide, precision=highest, preferred_element_type=jnp.float32).astype(jnp.bfloat16)
```

```python
import jax
import jax.numpy as jnp
from jax import lax
from jax.sharding import PartitionSpec as P

DEGREE = 4
NS_ITERS = 4


def from_behind(shard, axis, by):
    peers = lax.axis_size(axis)
    return lax.ppermute(shard, axis, [(i, (i + by) % peers) for i in range(peers)])


def apply_filter(wave_block, cell_matrices, connectivity, owner_list):
    column_count = wave_block.shape[0]
    node_count = wave_block.shape[1]
    plane_count = owner_list.shape[0]
    own_plane = jnp.take(wave_block, owner_list, axis=1)
    upper_plane = from_behind(own_plane, "space", -1)
    extended = jnp.concatenate([wave_block, upper_plane], axis=1)
    gathered = jnp.take(extended, connectivity, axis=1)
    products = jnp.einsum(
        "bcn,cnm->bcm", gathered, cell_matrices, preferred_element_type=jnp.float32
    )
    flat_index = connectivity.reshape(-1)
    summed = jnp.zeros((column_count, node_count + plane_count), jnp.float32)
    summed = summed.at[:, flat_index].add(products.reshape(column_count, flat_index.shape[0]))
    returned = from_behind(summed[:, node_count:], "space", 1)
    return summed[:, :node_count].at[:, owner_list].add(returned)


def butterfly_sum(block, axis):
    peers = lax.axis_size(axis)
    stride = 1
    while stride < peers:
        block = block + lax.ppermute(block, axis, [(i, i ^ stride) for i in range(peers)])
        stride *= 2
    return block


def newton_schulz(margin):
    highest = lax.Precision.HIGHEST
    size_cols = margin.shape[0]
    scale = jnp.sqrt(jnp.sum(margin * margin) + 1e-06)
    approx = margin / scale
    identity = jnp.eye(size_cols, dtype=jnp.float32)
    inverse = identity
    for iteration in range(NS_ITERS):
        middle = 1.5 * identity - 0.5 * jnp.dot(
            inverse, approx, precision=highest, preferred_element_type=jnp.float32
        )
        approx = jnp.dot(approx, middle, precision=highest, preferred_element_type=jnp.float32)
        inverse = jnp.dot(middle, inverse, precision=highest, preferred_element_type=jnp.float32)
    return (inverse / jnp.sqrt(scale)).astype(jnp.bfloat16)


def body(wavefunctions, filter_cells, connectivity, owner_list):
    previous = wavefunctions.astype(jnp.float32)
    current = apply_filter(wavefunctions, filter_cells, connectivity, owner_list)
    for degree_step in range(DEGREE - 1):
        following = (
            2.0 * apply_filter(current.astype(jnp.bfloat16), filter_cells, connectivity, owner_list)
            - previous
        )
        previous, current = (current, following)
    filtered = current.astype(jnp.bfloat16)
    node_total = filtered.shape[1] * lax.axis_size("space")
    column_count = filtered.shape[0]
    every_column = lax.all_gather(filtered, "wave", axis=0, tiled=True)
    own_rows = jnp.dot(filtered, every_column.T, preferred_element_type=jnp.float32)
    own_rows = butterfly_sum(own_rows, "space")
    margin = lax.all_gather(own_rows, "wave", axis=0, tiled=True) / node_total
    rotation = newton_schulz(margin)
    own_rotation = lax.dynamic_slice_in_dim(
        rotation, lax.axis_index("wave") * column_count, column_count, 1
    )
    return jnp.dot(own_rotation.T, every_column, preferred_element_type=jnp.float32).astype(
        jnp.bfloat16
    )


def solution(mesh):
    return jax.shard_map(
        body,
        mesh=mesh,
        in_specs=(P("wave", "space"), P("space", None, None), P("space", None), P("space")),
        out_specs=P("wave", "space"),
        check_vma=False,
    )
```

```python
import jax
import jax.numpy as jnp
from jax import lax
from jax.sharding import PartitionSpec as P

DEGREE = 4
NS_ITERS = 4


def from_behind(shard, axis, by):
    peers = lax.axis_size(axis)
    return lax.ppermute(shard, axis, [(i, (i + by) % peers) for i in range(peers)])


def split_three(values):
    pieces = []
    rest = values
    for piece in range(3):
        head = lax.reduce_precision(rest, exponent_bits=8, mantissa_bits=7)
        pieces.append(head.astype(jnp.bfloat16))
        rest = rest - head
    return jnp.concatenate(pieces, axis=0)


def sum_three(stacked):
    rows = stacked.shape[0] // 3
    return (stacked[:rows] + stacked[rows : 2 * rows]) + stacked[2 * rows :]


def selectors(connectivity, owner_list, node_count):
    plane_count = owner_list.shape[0]
    slots = jnp.arange(node_count + plane_count, dtype=connectivity.dtype)
    pick = (connectivity.reshape(-1)[:, None] == slots[None, :]).astype(jnp.bfloat16)
    owner = (slots[:node_count, None] == owner_list[None, :]).astype(jnp.bfloat16)
    return pick, owner


def apply_filter(wave_block, cell_matrices, pick, owner):
    column_count = wave_block.shape[0]
    node_count = wave_block.shape[1]
    cell_count, cell_nodes, _ = cell_matrices.shape
    own_plane = jnp.dot(wave_block, owner, preferred_element_type=jnp.float32).astype(jnp.bfloat16)
    upper_plane = from_behind(own_plane, "space", -1)
    contract_nodes = (((1,), (1,)), ((), ()))
    gathered = lax.dot_general(
        wave_block, pick[:, :node_count], contract_nodes, preferred_element_type=jnp.float32
    ) + lax.dot_general(
        upper_plane, pick[:, node_count:], contract_nodes, preferred_element_type=jnp.float32
    )
    gathered = gathered.astype(jnp.bfloat16).reshape(column_count, cell_count, cell_nodes)
    products = jnp.einsum(
        "bcn,cnm->bcm", gathered, cell_matrices, preferred_element_type=jnp.float32
    )
    stacked = split_three(products.reshape(column_count, cell_count * cell_nodes))
    plane_part = sum_three(
        jnp.dot(stacked, pick[:, node_count:], preferred_element_type=jnp.float32)
    )
    returned = from_behind(plane_part, "space", 1)
    local_part = sum_three(
        jnp.dot(stacked, pick[:, :node_count], preferred_element_type=jnp.float32)
    )
    back = sum_three(
        lax.dot_general(split_three(returned), owner, contract_nodes, preferred_element_type=jnp.float32)
    )
    return local_part + back


def butterfly_sum(block, axis):
    peers = lax.axis_size(axis)
    stride = 1
    while stride < peers:
        block = block + lax.ppermute(block, axis, [(i, i ^ stride) for i in range(peers)])
        stride *= 2
    return block


def newton_schulz(margin):
    highest = lax.Precision.HIGHEST
    size_cols = margin.shape[0]
    scale = jnp.sqrt(jnp.sum(margin * margin) + 1e-06)
    approx = margin / scale
    identity = jnp.eye(size_cols, dtype=jnp.float32)
    inverse = identity
    for iteration in range(NS_ITERS):
        middle = 1.5 * identity - 0.5 * jnp.dot(
            inverse, approx, precision=highest, preferred_element_type=jnp.float32
        )
        approx = jnp.dot(approx, middle, precision=highest, preferred_element_type=jnp.float32)
        inverse = jnp.dot(middle, inverse, precision=highest, preferred_element_type=jnp.float32)
    return (inverse / jnp.sqrt(scale)).astype(jnp.bfloat16)


def body(wavefunctions, filter_cells, connectivity, owner_list):
    pick, owner = selectors(connectivity, owner_list, wavefunctions.shape[1])
    previous = wavefunctions.astype(jnp.float32)
    current = apply_filter(wavefunctions, filter_cells, pick, owner)
    for degree_step in range(DEGREE - 1):
        following = (
            2.0 * apply_filter(current.astype(jnp.bfloat16), filter_cells, pick, owner)
            - previous
        )
        previous, current = (current, following)
    filtered = current.astype(jnp.bfloat16)
    node_total = filtered.shape[1] * lax.axis_size("space")
    column_count = filtered.shape[0]
    every_column = lax.all_gather(filtered, "wave", axis=0, tiled=True)
    own_rows = jnp.dot(filtered, every_column.T, preferred_element_type=jnp.float32)
    own_rows = butterfly_sum(own_rows, "space")
    margin = lax.all_gather(own_rows, "wave", axis=0, tiled=True) / node_total
    rotation = newton_schulz(margin)
    own_rotation = lax.dynamic_slice_in_dim(
        rotation, lax.axis_index("wave") * column_count, column_count, 1
    )
    return jnp.dot(own_rotation.T, every_column, preferred_element_type=jnp.float32).astype(
        jnp.bfloat16
    )


def solution(mesh):
    return jax.shard_map(
        body,
        mesh=mesh,
        in_specs=(P("wave", "space"), P("space", None, None), P("space", None), P("space")),
        out_specs=P("wave", "space"),
        check_vma=False,
    )
```

```python
import jax
import jax.numpy as jnp
from jax import lax
from jax.sharding import PartitionSpec as P

DEGREE = 4
NS_ITERS = 4


def from_behind(shard, axis, by):
    peers = lax.axis_size(axis)
    return lax.ppermute(shard, axis, [(i, (i + by) % peers) for i in range(peers)])


def split_three(values):
    pieces = []
    rest = values
    for piece in range(3):
        head = lax.reduce_precision(rest, exponent_bits=8, mantissa_bits=7)
        pieces.append(head.astype(jnp.bfloat16))
        rest = rest - head
    return jnp.concatenate(pieces, axis=0)


def sum_three(stacked):
    rows = stacked.shape[0] // 3
    return (stacked[:rows] + stacked[rows : 2 * rows]) + stacked[2 * rows :]


def selectors(connectivity, owner_list, node_count):
    plane_count = owner_list.shape[0]
    slots = jnp.arange(node_count + plane_count, dtype=connectivity.dtype)
    pick = (connectivity.reshape(-1)[:, None] == slots[None, :]).astype(jnp.bfloat16)
    owner = (slots[:node_count, None] == owner_list[None, :]).astype(jnp.bfloat16)
    return pick, owner


def apply_filter(wave_block, cell_matrices, pick, owner):
    column_count = wave_block.shape[0]
    node_count = wave_block.shape[1]
    cell_count, cell_nodes, _ = cell_matrices.shape
    own_plane = jnp.dot(wave_block, owner, preferred_element_type=jnp.float32).astype(jnp.bfloat16)
    upper_plane = from_behind(own_plane, "space", -1)
    contract_nodes = (((1,), (1,)), ((), ()))
    gathered = lax.dot_general(
        wave_block, pick[:, :node_count], contract_nodes, preferred_element_type=jnp.float32
    ) + lax.dot_general(
        upper_plane, pick[:, node_count:], contract_nodes, preferred_element_type=jnp.float32
    )
    gathered = gathered.astype(jnp.bfloat16).reshape(column_count, cell_count, cell_nodes)
    products = jnp.einsum(
        "bcn,cnm->bcm", gathered, cell_matrices, preferred_element_type=jnp.float32
    )
    stacked = split_three(products.reshape(column_count, cell_count * cell_nodes))
    plane_part = sum_three(
        jnp.dot(stacked, pick[:, node_count:], preferred_element_type=jnp.float32)
    )
    returned = from_behind(plane_part, "space", 1)
    local_part = sum_three(
        jnp.dot(stacked, pick[:, :node_count], preferred_element_type=jnp.float32)
    )
    back = sum_three(
        lax.dot_general(split_three(returned), owner, contract_nodes, preferred_element_type=jnp.float32)
    )
    return local_part + back


def butterfly_sum(block, axis, spread):
    peers = lax.axis_size(axis)
    me = lax.axis_index(axis)

    def partner(stride):
        return [(i, i ^ stride) for i in range(peers)]

    rows = block
    stride = 1
    while stride < spread:
        half = rows.shape[0] // 2
        upper = (me // stride) % 2 == 1
        keep = jnp.where(upper, rows[half:], rows[:half])
        send = jnp.where(upper, rows[:half], rows[half:])
        rows = keep + lax.ppermute(send, axis, partner(stride))
        stride *= 2
    while stride < peers:
        rows = rows + lax.ppermute(rows, axis, partner(stride))
        stride *= 2
    stride = spread // 2
    while stride >= 1:
        upper = (me // stride) % 2 == 1
        other = lax.ppermute(rows, axis, partner(stride))
        rows = jnp.where(
            upper,
            jnp.concatenate([other, rows], axis=0),
            jnp.concatenate([rows, other], axis=0),
        )
        stride //= 2
    return rows


def newton_schulz(margin):
    highest = lax.Precision.HIGHEST
    size_cols = margin.shape[0]
    scale = jnp.sqrt(jnp.sum(margin * margin) + 1e-06)
    approx = margin / scale
    identity = jnp.eye(size_cols, dtype=jnp.float32)
    inverse = identity
    for iteration in range(NS_ITERS):
        middle = 1.5 * identity - 0.5 * jnp.dot(
            inverse, approx, precision=highest, preferred_element_type=jnp.float32
        )
        approx = jnp.dot(approx, middle, precision=highest, preferred_element_type=jnp.float32)
        inverse = jnp.dot(middle, inverse, precision=highest, preferred_element_type=jnp.float32)
    return (inverse / jnp.sqrt(scale)).astype(jnp.bfloat16)


def body(wavefunctions, filter_cells, connectivity, owner_list):
    pick, owner = selectors(connectivity, owner_list, wavefunctions.shape[1])
    previous = wavefunctions.astype(jnp.float32)
    current = apply_filter(wavefunctions, filter_cells, pick, owner)
    for degree_step in range(DEGREE - 1):
        following = (
            2.0 * apply_filter(current.astype(jnp.bfloat16), filter_cells, pick, owner)
            - previous
        )
        previous, current = (current, following)
    filtered = current.astype(jnp.bfloat16)
    node_total = filtered.shape[1] * lax.axis_size("space")
    column_count = filtered.shape[0]
    every_column = lax.all_gather(filtered, "wave", axis=0, tiled=True)
    own_rows = jnp.dot(filtered, every_column.T, preferred_element_type=jnp.float32)
    own_rows = butterfly_sum(own_rows, "space", 4)
    margin = lax.all_gather(own_rows, "wave", axis=0, tiled=True) / node_total
    rotation = newton_schulz(margin)
    own_rotation = lax.dynamic_slice_in_dim(
        rotation, lax.axis_index("wave") * column_count, column_count, 1
    )
    return jnp.dot(own_rotation.T, every_column, preferred_element_type=jnp.float32).astype(
        jnp.bfloat16
    )


def solution(mesh):
    return jax.shard_map(
        body,
        mesh=mesh,
        in_specs=(P("wave", "space"), P("space", None, None), P("space", None), P("space")),
        out_specs=P("wave", "space"),
        check_vma=False,
    )
```

```python
import jax
import jax.numpy as jnp
from jax import lax
from jax.sharding import PartitionSpec as P

DEGREE = 4
NS_ITERS = 4


def from_behind(shard, axis, by):
    peers = lax.axis_size(axis)
    return lax.ppermute(shard, axis, [(i, (i + by) % peers) for i in range(peers)])


def split_three(values):
    pieces = []
    rest = values
    for piece in range(3):
        head = lax.reduce_precision(rest, exponent_bits=8, mantissa_bits=7)
        pieces.append(head.astype(jnp.bfloat16))
        rest = rest - head
    return jnp.concatenate(pieces, axis=0)


def sum_three(stacked):
    rows = stacked.shape[0] // 3
    return (stacked[:rows] + stacked[rows : 2 * rows]) + stacked[2 * rows :]


def selectors(connectivity, owner_list, node_count):
    plane_count = owner_list.shape[0]
    slots = jnp.arange(node_count + plane_count, dtype=connectivity.dtype)
    pick = (connectivity.reshape(-1)[:, None] == slots[None, :]).astype(jnp.bfloat16)
    owner = (slots[:node_count, None] == owner_list[None, :]).astype(jnp.bfloat16)
    return pick, owner


def plane_coupling(cell_matrices, pick, node_count):
    cell_count, cell_nodes, _ = cell_matrices.shape
    plane_pick = pick[:, node_count:]
    per_cell = plane_pick.reshape(cell_count, cell_nodes, plane_pick.shape[1])
    halfway = jnp.einsum("clq,clm->qcm", per_cell, cell_matrices, preferred_element_type=jnp.float32)
    halfway = halfway.reshape(plane_pick.shape[1], cell_count * cell_nodes)
    coupling = sum_three(jnp.dot(split_three(halfway), plane_pick, preferred_element_type=jnp.float32))
    return from_behind(split_three(coupling), "space", 1)


def apply_filter(wave_block, cell_matrices, pick, owner, coupling_below):
    column_count = wave_block.shape[0]
    node_count = wave_block.shape[1]
    cell_count, cell_nodes, _ = cell_matrices.shape
    plane_count = owner.shape[1]
    contract_nodes = (((1,), (1,)), ((), ()))
    own_plane = jnp.dot(wave_block, owner, preferred_element_type=jnp.float32).astype(jnp.bfloat16)
    upper_plane = from_behind(own_plane, "space", -1)
    from_own = lax.dot_general(
        wave_block, pick[:, :node_count], contract_nodes, preferred_element_type=jnp.float32
    ).astype(jnp.bfloat16)
    own_products = jnp.einsum(
        "bcn,cnm->bcm",
        from_own.reshape(column_count, cell_count, cell_nodes),
        cell_matrices,
        preferred_element_type=jnp.float32,
    )
    sent_up = sum_three(
        jnp.dot(
            split_three(own_products.reshape(column_count, cell_count * cell_nodes)),
            pick[:, node_count:],
            preferred_element_type=jnp.float32,
        )
    )
    received = from_behind(sent_up, "space", 1)
    from_upper = lax.dot_general(
        upper_plane, pick[:, node_count:], contract_nodes, preferred_element_type=jnp.float32
    ).astype(jnp.bfloat16)
    products = jnp.einsum(
        "bcn,cnm->bcm",
        (from_own + from_upper).reshape(column_count, cell_count, cell_nodes),
        cell_matrices,
        preferred_element_type=jnp.float32,
    )
    local_part = sum_three(
        jnp.dot(
            split_three(products.reshape(column_count, cell_count * cell_nodes)),
            pick[:, :node_count],
            preferred_element_type=jnp.float32,
        )
    )
    pieces = coupling_below.reshape(3, plane_count, plane_count)
    coupled = jnp.einsum("bq,kqp->kbp", own_plane, pieces, preferred_element_type=jnp.float32)
    plane_total = received + ((coupled[0] + coupled[1]) + coupled[2])
    back = sum_three(
        lax.dot_general(split_three(plane_total), owner, contract_nodes, preferred_element_type=jnp.float32)
    )
    return local_part + back


def butterfly_sum(block, axis):
    peers = lax.axis_size(axis)
    stride = 1
    while stride < peers:
        block = block + lax.ppermute(block, axis, [(i, i ^ stride) for i in range(peers)])
        stride *= 2
    return block


def newton_schulz(margin):
    highest = lax.Precision.HIGHEST
    size_cols = margin.shape[0]
    scale = jnp.sqrt(jnp.sum(margin * margin) + 1e-06)
    approx = margin / scale
    identity = jnp.eye(size_cols, dtype=jnp.float32)
    inverse = identity
    for iteration in range(NS_ITERS):
        middle = 1.5 * identity - 0.5 * jnp.dot(
            inverse, approx, precision=highest, preferred_element_type=jnp.float32
        )
        approx = jnp.dot(approx, middle, precision=highest, preferred_element_type=jnp.float32)
        inverse = jnp.dot(middle, inverse, precision=highest, preferred_element_type=jnp.float32)
    return (inverse / jnp.sqrt(scale)).astype(jnp.bfloat16)


def body(wavefunctions, filter_cells, connectivity, owner_list):
    pick, owner = selectors(connectivity, owner_list, wavefunctions.shape[1])
    coupling_below = plane_coupling(filter_cells, pick, wavefunctions.shape[1])
    previous = wavefunctions.astype(jnp.float32)
    current = apply_filter(wavefunctions, filter_cells, pick, owner, coupling_below)
    for degree_step in range(DEGREE - 1):
        following = (
            2.0
            * apply_filter(current.astype(jnp.bfloat16), filter_cells, pick, owner, coupling_below)
            - previous
        )
        previous, current = (current, following)
    filtered = current.astype(jnp.bfloat16)
    node_total = filtered.shape[1] * lax.axis_size("space")
    column_count = filtered.shape[0]
    every_column = lax.all_gather(filtered, "wave", axis=0, tiled=True)
    own_rows = jnp.dot(filtered, every_column.T, preferred_element_type=jnp.float32)
    own_rows = butterfly_sum(own_rows, "space")
    margin = lax.all_gather(own_rows, "wave", axis=0, tiled=True) / node_total
    rotation = newton_schulz(margin)
    own_rotation = lax.dynamic_slice_in_dim(
        rotation, lax.axis_index("wave") * column_count, column_count, 1
    )
    return jnp.dot(own_rotation.T, every_column, preferred_element_type=jnp.float32).astype(
        jnp.bfloat16
    )


def solution(mesh):
    return jax.shard_map(
        body,
        mesh=mesh,
        in_specs=(P("wave", "space"), P("space", None, None), P("space", None), P("space")),
        out_specs=P("wave", "space"),
        check_vma=False,
    )
```

```python
import jax
import jax.numpy as jnp
from jax import lax
from jax.sharding import PartitionSpec as P

DEGREE = 4
NS_ITERS = 4


def from_behind(shard, axis, by):
    peers = lax.axis_size(axis)
    return lax.ppermute(shard, axis, [(i, (i + by) % peers) for i in range(peers)])


def split_three(values):
    pieces = []
    rest = values
    for piece in range(3):
        head = lax.reduce_precision(rest, exponent_bits=8, mantissa_bits=7)
        pieces.append(head.astype(jnp.bfloat16))
        rest = rest - head
    return jnp.concatenate(pieces, axis=0)


def sum_three(stacked):
    rows = stacked.shape[0] // 3
    return (stacked[:rows] + stacked[rows : 2 * rows]) + stacked[2 * rows :]


def selectors(connectivity, owner_list, node_count):
    plane_count = owner_list.shape[0]
    slots = jnp.arange(node_count + plane_count, dtype=connectivity.dtype)
    pick = (connectivity.reshape(-1)[:, None] == slots[None, :]).astype(jnp.bfloat16)
    owner = (slots[:node_count, None] == owner_list[None, :]).astype(jnp.bfloat16)
    return pick, owner


def apply_filter(wave_block, cell_matrices, pick, owner):
    column_count = wave_block.shape[0]
    node_count = wave_block.shape[1]
    cell_count, cell_nodes, _ = cell_matrices.shape
    own_plane = jnp.dot(wave_block, owner, preferred_element_type=jnp.float32).astype(jnp.bfloat16)
    upper_plane = from_behind(own_plane, "space", -1)
    contract_nodes = (((1,), (1,)), ((), ()))
    gathered = lax.dot_general(
        wave_block, pick[:, :node_count], contract_nodes, preferred_element_type=jnp.float32
    ) + lax.dot_general(
        upper_plane, pick[:, node_count:], contract_nodes, preferred_element_type=jnp.float32
    )
    gathered = gathered.astype(jnp.bfloat16).reshape(column_count, cell_count, cell_nodes)
    products = jnp.einsum(
        "bcn,cnm->bcm", gathered, cell_matrices, preferred_element_type=jnp.float32
    )
    stacked = split_three(products.reshape(column_count, cell_count * cell_nodes))
    plane_part = sum_three(
        jnp.dot(stacked, pick[:, node_count:], preferred_element_type=jnp.float32)
    )
    returned = from_behind(plane_part, "space", 1)
    local_part = sum_three(
        jnp.dot(stacked, pick[:, :node_count], preferred_element_type=jnp.float32)
    )
    back = sum_three(
        lax.dot_general(split_three(returned), owner, contract_nodes, preferred_element_type=jnp.float32)
    )
    return local_part + back


def ring_partners(count):
    steps = []
    stride = 1
    while stride * 2 < count:
        steps.append([position ^ stride for position in range(count)])
        stride *= 2
    quarter = count // 4
    if count >= 4:
        steps.append(
            [
                (position + quarter) % count if (position // quarter) % 2 else (position - quarter) % count
                for position in range(count)
            ]
        )
    elif count == 2:
        steps.append([1, 0])
    return steps


def butterfly_sum(block, axis, inner):
    peers = lax.axis_size(axis)
    outer = peers // inner
    for step in ring_partners(inner):
        pairs = [(i, (i // inner) * inner + step[i % inner]) for i in range(peers)]
        block = block + lax.ppermute(block, axis, pairs)
    for step in ring_partners(outer):
        pairs = [(i, step[i // inner] * inner + i % inner) for i in range(peers)]
        block = block + lax.ppermute(block, axis, pairs)
    return block


def newton_schulz(margin):
    highest = lax.Precision.HIGHEST
    size_cols = margin.shape[0]
    scale = jnp.sqrt(jnp.sum(margin * margin) + 1e-06)
    approx = margin / scale
    identity = jnp.eye(size_cols, dtype=jnp.float32)
    inverse = identity
    for iteration in range(NS_ITERS):
        middle = 1.5 * identity - 0.5 * jnp.dot(
            inverse, approx, precision=highest, preferred_element_type=jnp.float32
        )
        approx = jnp.dot(approx, middle, precision=highest, preferred_element_type=jnp.float32)
        inverse = jnp.dot(middle, inverse, precision=highest, preferred_element_type=jnp.float32)
    return (inverse / jnp.sqrt(scale)).astype(jnp.bfloat16)


def body(wavefunctions, filter_cells, connectivity, owner_list):
    pick, owner = selectors(connectivity, owner_list, wavefunctions.shape[1])
    previous = wavefunctions.astype(jnp.float32)
    current = apply_filter(wavefunctions, filter_cells, pick, owner)
    for degree_step in range(DEGREE - 1):
        following = (
            2.0 * apply_filter(current.astype(jnp.bfloat16), filter_cells, pick, owner)
            - previous
        )
        previous, current = (current, following)
    filtered = current.astype(jnp.bfloat16)
    node_total = filtered.shape[1] * lax.axis_size("space")
    column_count = filtered.shape[0]
    every_column = lax.all_gather(filtered, "wave", axis=0, tiled=True)
    own_rows = jnp.dot(filtered, every_column.T, preferred_element_type=jnp.float32)
    own_rows = butterfly_sum(own_rows, "space", 4)
    margin = lax.all_gather(own_rows, "wave", axis=0, tiled=True) / node_total
    rotation = newton_schulz(margin)
    own_rotation = lax.dynamic_slice_in_dim(
        rotation, lax.axis_index("wave") * column_count, column_count, 1
    )
    return jnp.dot(own_rotation.T, every_column, preferred_element_type=jnp.float32).astype(
        jnp.bfloat16
    )


def solution(mesh):
    return jax.shard_map(
        body,
        mesh=mesh,
        in_specs=(P("wave", "space"), P("space", None, None), P("space", None), P("space")),
        out_specs=P("wave", "space"),
        check_vma=False,
    )
```

```python
import jax
import jax.numpy as jnp
from jax import lax
from jax.sharding import PartitionSpec as P

DEGREE = 4
NS_ITERS = 4


def from_behind(shard, axis, by):
    peers = lax.axis_size(axis)
    return lax.ppermute(shard, axis, [(i, (i + by) % peers) for i in range(peers)])


def split_three(values):
    pieces = []
    rest = values
    for piece in range(3):
        head = lax.reduce_precision(rest, exponent_bits=8, mantissa_bits=7)
        pieces.append(head.astype(jnp.bfloat16))
        rest = rest - head
    return jnp.concatenate(pieces, axis=0)


def sum_three(stacked):
    rows = stacked.shape[0] // 3
    return (stacked[:rows] + stacked[rows : 2 * rows]) + stacked[2 * rows :]


def selectors(connectivity, owner_list, node_count):
    plane_count = owner_list.shape[0]
    slots = jnp.arange(node_count + plane_count, dtype=connectivity.dtype)
    pick = (connectivity.reshape(-1)[:, None] == slots[None, :]).astype(jnp.bfloat16)
    owner = (slots[:node_count, None] == owner_list[None, :]).astype(jnp.bfloat16)
    return pick, owner


def apply_filter(wave_block, own_plane, cell_matrices, pick, owner):
    column_count = wave_block.shape[0]
    node_count = wave_block.shape[1]
    cell_count, cell_nodes, _ = cell_matrices.shape
    upper_plane = from_behind(own_plane, "space", -1)
    contract_nodes = (((1,), (1,)), ((), ()))
    gathered = lax.dot_general(
        wave_block, pick[:, :node_count], contract_nodes, preferred_element_type=jnp.float32
    ) + lax.dot_general(
        upper_plane, pick[:, node_count:], contract_nodes, preferred_element_type=jnp.float32
    )
    gathered = gathered.astype(jnp.bfloat16).reshape(column_count, cell_count, cell_nodes)
    products = jnp.einsum(
        "bcn,cnm->bcm", gathered, cell_matrices, preferred_element_type=jnp.float32
    )
    stacked = split_three(products.reshape(column_count, cell_count * cell_nodes))
    plane_part = sum_three(
        jnp.dot(stacked, pick[:, node_count:], preferred_element_type=jnp.float32)
    )
    returned = from_behind(plane_part, "space", 1)
    local_part = sum_three(
        jnp.dot(stacked, pick[:, :node_count], preferred_element_type=jnp.float32)
    )
    local_plane = sum_three(
        jnp.dot(split_three(local_part), owner, preferred_element_type=jnp.float32)
    )
    back = sum_three(
        lax.dot_general(split_three(returned), owner, contract_nodes, preferred_element_type=jnp.float32)
    )
    return local_part + back, local_plane + returned


def ring_partners(count):
    steps = []
    stride = 1
    while stride * 2 < count:
        steps.append([position ^ stride for position in range(count)])
        stride *= 2
    quarter = count // 4
    if count >= 4:
        steps.append(
            [
                (position + quarter) % count if (position // quarter) % 2 else (position - quarter) % count
                for position in range(count)
            ]
        )
    elif count == 2:
        steps.append([1, 0])
    return steps


def butterfly_sum(block, axis, inner):
    peers = lax.axis_size(axis)
    outer = peers // inner
    for step in ring_partners(inner):
        pairs = [(i, (i // inner) * inner + step[i % inner]) for i in range(peers)]
        block = block + lax.ppermute(block, axis, pairs)
    for step in ring_partners(outer):
        pairs = [(i, step[i // inner] * inner + i % inner) for i in range(peers)]
        block = block + lax.ppermute(block, axis, pairs)
    return block


def newton_schulz(margin):
    highest = lax.Precision.HIGHEST
    size_cols = margin.shape[0]
    scale = jnp.sqrt(jnp.sum(margin * margin) + 1e-06)
    approx = margin / scale
    identity = jnp.eye(size_cols, dtype=jnp.float32)
    inverse = identity
    for iteration in range(NS_ITERS):
        middle = 1.5 * identity - 0.5 * jnp.dot(
            inverse, approx, precision=highest, preferred_element_type=jnp.float32
        )
        approx = jnp.dot(approx, middle, precision=highest, preferred_element_type=jnp.float32)
        inverse = jnp.dot(middle, inverse, precision=highest, preferred_element_type=jnp.float32)
    return (inverse / jnp.sqrt(scale)).astype(jnp.bfloat16)


def body(wavefunctions, filter_cells, connectivity, owner_list):
    pick, owner = selectors(connectivity, owner_list, wavefunctions.shape[1])
    start_plane = jnp.dot(wavefunctions, owner, preferred_element_type=jnp.float32).astype(jnp.bfloat16)
    previous = wavefunctions.astype(jnp.float32)
    previous_plane = start_plane.astype(jnp.float32)
    current, current_plane = apply_filter(wavefunctions, start_plane, filter_cells, pick, owner)
    for degree_step in range(DEGREE - 1):
        applied, applied_plane = apply_filter(
            current.astype(jnp.bfloat16), current_plane.astype(jnp.bfloat16), filter_cells, pick, owner
        )
        following = 2.0 * applied - previous
        following_plane = 2.0 * applied_plane - previous_plane
        previous, current = (current, following)
        previous_plane, current_plane = (current_plane, following_plane)
    filtered = current.astype(jnp.bfloat16)
    node_total = filtered.shape[1] * lax.axis_size("space")
    column_count = filtered.shape[0]
    every_column = lax.all_gather(filtered, "wave", axis=0, tiled=True)
    own_rows = jnp.dot(filtered, every_column.T, preferred_element_type=jnp.float32)
    own_rows = butterfly_sum(own_rows, "space", 4)
    margin = lax.all_gather(own_rows, "wave", axis=0, tiled=True) / node_total
    rotation = newton_schulz(margin)
    own_rotation = lax.dynamic_slice_in_dim(
        rotation, lax.axis_index("wave") * column_count, column_count, 1
    )
    return jnp.dot(own_rotation.T, every_column, preferred_element_type=jnp.float32).astype(
        jnp.bfloat16
    )


def solution(mesh):
    return jax.shard_map(
        body,
        mesh=mesh,
        in_specs=(P("wave", "space"), P("space", None, None), P("space", None), P("space")),
        out_specs=P("wave", "space"),
        check_vma=False,
    )
```

```python
import jax
import jax.numpy as jnp
from jax import lax
from jax.sharding import PartitionSpec as P

DEGREE = 4
NS_ITERS = 4


def from_behind(shard, axis, by):
    peers = lax.axis_size(axis)
    return lax.ppermute(shard, axis, [(i, (i + by) % peers) for i in range(peers)])


def split_three(values):
    pieces = []
    rest = values
    for piece in range(3):
        head = lax.reduce_precision(rest, exponent_bits=8, mantissa_bits=7)
        pieces.append(head.astype(jnp.bfloat16))
        rest = rest - head
    return jnp.concatenate(pieces, axis=0)


def sum_three(stacked):
    rows = stacked.shape[0] // 3
    return (stacked[:rows] + stacked[rows : 2 * rows]) + stacked[2 * rows :]


def selectors(connectivity, owner_list, node_count):
    plane_count = owner_list.shape[0]
    slots = jnp.arange(node_count + plane_count, dtype=connectivity.dtype)
    pick = (connectivity.reshape(-1)[:, None] == slots[None, :]).astype(jnp.bfloat16)
    owner = (slots[:node_count, None] == owner_list[None, :]).astype(jnp.bfloat16)
    return pick, owner


def plane_coupling(cell_matrices, pick, node_count):
    cell_count, cell_nodes, _ = cell_matrices.shape
    plane_pick = pick[:, node_count:]
    plane_count = plane_pick.shape[1]
    per_cell = plane_pick.reshape(cell_count, cell_nodes, plane_count)
    halfway = jnp.einsum("clq,clm->qcm", per_cell, cell_matrices, preferred_element_type=jnp.float32)
    halfway = halfway.reshape(plane_count, cell_count * cell_nodes)
    coupling = sum_three(jnp.dot(split_three(halfway), plane_pick, preferred_element_type=jnp.float32))
    return split_three(coupling).reshape(3, plane_count, plane_count)


def apply_filter(wave_block, cell_matrices, pick, owner, coupling):
    column_count = wave_block.shape[0]
    node_count = wave_block.shape[1]
    cell_count, cell_nodes, _ = cell_matrices.shape
    contract_nodes = (((1,), (1,)), ((), ()))
    own_plane = jnp.dot(wave_block, owner, preferred_element_type=jnp.float32).astype(jnp.bfloat16)
    upper_plane = from_behind(own_plane, "space", -1)
    from_own = lax.dot_general(
        wave_block, pick[:, :node_count], contract_nodes, preferred_element_type=jnp.float32
    ).astype(jnp.bfloat16)
    own_products = jnp.einsum(
        "bcn,cnm->bcm",
        from_own.reshape(column_count, cell_count, cell_nodes),
        cell_matrices,
        preferred_element_type=jnp.float32,
    )
    from_own_nodes = sum_three(
        jnp.dot(
            split_three(own_products.reshape(column_count, cell_count * cell_nodes)),
            pick[:, node_count:],
            preferred_element_type=jnp.float32,
        )
    )
    coupled = jnp.einsum("bq,kqp->kbp", upper_plane, coupling, preferred_element_type=jnp.float32)
    plane_part = from_own_nodes + ((coupled[0] + coupled[1]) + coupled[2])
    returned = from_behind(plane_part, "space", 1)
    from_upper = lax.dot_general(
        upper_plane, pick[:, node_count:], contract_nodes, preferred_element_type=jnp.float32
    ).astype(jnp.bfloat16)
    products = jnp.einsum(
        "bcn,cnm->bcm",
        (from_own + from_upper).reshape(column_count, cell_count, cell_nodes),
        cell_matrices,
        preferred_element_type=jnp.float32,
    )
    local_part = sum_three(
        jnp.dot(
            split_three(products.reshape(column_count, cell_count * cell_nodes)),
            pick[:, :node_count],
            preferred_element_type=jnp.float32,
        )
    )
    back = sum_three(
        lax.dot_general(split_three(returned), owner, contract_nodes, preferred_element_type=jnp.float32)
    )
    return local_part + back


def ring_partners(count):
    steps = []
    stride = 1
    while stride * 2 < count:
        steps.append([position ^ stride for position in range(count)])
        stride *= 2
    quarter = count // 4
    if count >= 4:
        steps.append(
            [
                (position + quarter) % count if (position // quarter) % 2 else (position - quarter) % count
                for position in range(count)
            ]
        )
    elif count == 2:
        steps.append([1, 0])
    return steps


def butterfly_sum(block, axis, inner):
    peers = lax.axis_size(axis)
    outer = peers // inner
    for step in ring_partners(inner):
        pairs = [(i, (i // inner) * inner + step[i % inner]) for i in range(peers)]
        block = block + lax.ppermute(block, axis, pairs)
    for step in ring_partners(outer):
        pairs = [(i, step[i // inner] * inner + i % inner) for i in range(peers)]
        block = block + lax.ppermute(block, axis, pairs)
    return block


def newton_schulz(margin):
    highest = lax.Precision.HIGHEST
    size_cols = margin.shape[0]
    scale = jnp.sqrt(jnp.sum(margin * margin) + 1e-06)
    approx = margin / scale
    identity = jnp.eye(size_cols, dtype=jnp.float32)
    inverse = identity
    for iteration in range(NS_ITERS):
        middle = 1.5 * identity - 0.5 * jnp.dot(
            inverse, approx, precision=highest, preferred_element_type=jnp.float32
        )
        approx = jnp.dot(approx, middle, precision=highest, preferred_element_type=jnp.float32)
        inverse = jnp.dot(middle, inverse, precision=highest, preferred_element_type=jnp.float32)
    return (inverse / jnp.sqrt(scale)).astype(jnp.bfloat16)


def body(wavefunctions, filter_cells, connectivity, owner_list):
    pick, owner = selectors(connectivity, owner_list, wavefunctions.shape[1])
    coupling = plane_coupling(filter_cells, pick, wavefunctions.shape[1])
    previous = wavefunctions.astype(jnp.float32)
    current = apply_filter(wavefunctions, filter_cells, pick, owner, coupling)
    for degree_step in range(DEGREE - 1):
        following = (
            2.0 * apply_filter(current.astype(jnp.bfloat16), filter_cells, pick, owner, coupling)
            - previous
        )
        previous, current = (current, following)
    filtered = current.astype(jnp.bfloat16)
    node_total = filtered.shape[1] * lax.axis_size("space")
    column_count = filtered.shape[0]
    every_column = lax.all_gather(filtered, "wave", axis=0, tiled=True)
    own_rows = jnp.dot(filtered, every_column.T, preferred_element_type=jnp.float32)
    own_rows = butterfly_sum(own_rows, "space", 4)
    margin = lax.all_gather(own_rows, "wave", axis=0, tiled=True) / node_total
    rotation = newton_schulz(margin)
    own_rotation = lax.dynamic_slice_in_dim(
        rotation, lax.axis_index("wave") * column_count, column_count, 1
    )
    return jnp.dot(own_rotation.T, every_column, preferred_element_type=jnp.float32).astype(
        jnp.bfloat16
    )


def solution(mesh):
    return jax.shard_map(
        body,
        mesh=mesh,
        in_specs=(P("wave", "space"), P("space", None, None), P("space", None), P("space")),
        out_specs=P("wave", "space"),
        check_vma=False,
    )
```

```python
import jax
import jax.numpy as jnp
from jax import lax
from jax.sharding import PartitionSpec as P

DEGREE = 4
NS_ITERS = 4


def from_behind(shard, axis, by):
    peers = lax.axis_size(axis)
    return lax.ppermute(shard, axis, [(i, (i + by) % peers) for i in range(peers)])


def split_three(values):
    pieces = []
    rest = values
    for piece in range(3):
        head = lax.reduce_precision(rest, exponent_bits=8, mantissa_bits=7)
        pieces.append(head.astype(jnp.bfloat16))
        rest = rest - head
    return jnp.concatenate(pieces, axis=0)


def sum_three(stacked):
    rows = stacked.shape[0] // 3
    return (stacked[:rows] + stacked[rows : 2 * rows]) + stacked[2 * rows :]


def selectors(connectivity, owner_list, node_count):
    plane_count = owner_list.shape[0]
    slots = jnp.arange(node_count + plane_count, dtype=connectivity.dtype)
    pick = (connectivity.reshape(-1)[:, None] == slots[None, :]).astype(jnp.bfloat16)
    owner = (slots[:node_count, None] == owner_list[None, :]).astype(jnp.bfloat16)
    return pick, owner


def apply_filter(wave_block, cell_matrices, pick, owner):
    column_count = wave_block.shape[0]
    node_count = wave_block.shape[1]
    cell_count, cell_nodes, _ = cell_matrices.shape
    own_plane = jnp.dot(wave_block, owner, preferred_element_type=jnp.float32).astype(jnp.bfloat16)
    upper_plane = from_behind(own_plane, "space", -1)
    contract_nodes = (((1,), (1,)), ((), ()))
    gathered = lax.dot_general(
        wave_block, pick[:, :node_count], contract_nodes, preferred_element_type=jnp.float32
    ) + lax.dot_general(
        upper_plane, pick[:, node_count:], contract_nodes, preferred_element_type=jnp.float32
    )
    gathered = gathered.astype(jnp.bfloat16).reshape(column_count, cell_count, cell_nodes)
    products = jnp.einsum(
        "bcn,cnm->bcm", gathered, cell_matrices, preferred_element_type=jnp.float32
    )
    stacked = split_three(products.reshape(column_count, cell_count * cell_nodes))
    plane_part = sum_three(
        jnp.dot(stacked, pick[:, node_count:], preferred_element_type=jnp.float32)
    )
    returned = from_behind(plane_part, "space", 1)
    local_part = sum_three(
        jnp.dot(stacked, pick[:, :node_count], preferred_element_type=jnp.float32)
    )
    back = sum_three(
        lax.dot_general(split_three(returned), owner, contract_nodes, preferred_element_type=jnp.float32)
    )
    return local_part + back


def ring_partners(count):
    steps = []
    stride = 1
    while stride * 2 < count:
        steps.append([position ^ stride for position in range(count)])
        stride *= 2
    quarter = count // 4
    if count >= 4:
        steps.append(
            [
                (position + quarter) % count if (position // quarter) % 2 else (position - quarter) % count
                for position in range(count)
            ]
        )
    elif count == 2:
        steps.append([1, 0])
    return steps


def butterfly_sum(block, axis, inner):
    peers = lax.axis_size(axis)
    outer = peers // inner
    for step in ring_partners(inner):
        pairs = [(i, (i // inner) * inner + step[i % inner]) for i in range(peers)]
        block = block + lax.ppermute(block, axis, pairs)
    for step in ring_partners(outer):
        pairs = [(i, step[i // inner] * inner + i % inner) for i in range(peers)]
        block = block + lax.ppermute(block, axis, pairs)
    return block


def newton_schulz(margin):
    highest = lax.Precision.HIGHEST
    size_cols = margin.shape[0]
    scale = jnp.sqrt(jnp.sum(margin * margin) + 1e-06)
    approx = margin / scale
    identity = jnp.eye(size_cols, dtype=jnp.float32)
    middle = 1.5 * identity - 0.5 * approx
    approx = jnp.dot(approx, middle, precision=highest, preferred_element_type=jnp.float32)
    inverse = middle
    for iteration in range(NS_ITERS - 1):
        middle = 1.5 * identity - 0.5 * jnp.dot(
            inverse, approx, precision=highest, preferred_element_type=jnp.float32
        )
        approx = jnp.dot(approx, middle, precision=highest, preferred_element_type=jnp.float32)
        inverse = jnp.dot(middle, inverse, precision=highest, preferred_element_type=jnp.float32)
    return (inverse / jnp.sqrt(scale)).astype(jnp.bfloat16)


def body(wavefunctions, filter_cells, connectivity, owner_list):
    pick, owner = selectors(connectivity, owner_list, wavefunctions.shape[1])
    previous = wavefunctions.astype(jnp.float32)
    current = apply_filter(wavefunctions, filter_cells, pick, owner)
    for degree_step in range(DEGREE - 1):
        following = (
            2.0 * apply_filter(current.astype(jnp.bfloat16), filter_cells, pick, owner)
            - previous
        )
        previous, current = (current, following)
    filtered = current.astype(jnp.bfloat16)
    node_total = filtered.shape[1] * lax.axis_size("space")
    column_count = filtered.shape[0]
    every_column = lax.all_gather(filtered, "wave", axis=0, tiled=True)
    own_rows = jnp.dot(filtered, every_column.T, preferred_element_type=jnp.float32)
    own_rows = butterfly_sum(own_rows, "space", 4)
    margin = lax.all_gather(own_rows, "wave", axis=0, tiled=True) / node_total
    rotation = newton_schulz(margin)
    own_rotation = lax.dynamic_slice_in_dim(
        rotation, lax.axis_index("wave") * column_count, column_count, 1
    )
    return jnp.dot(own_rotation.T, every_column, preferred_element_type=jnp.float32).astype(
        jnp.bfloat16
    )


def solution(mesh):
    return jax.shard_map(
        body,
        mesh=mesh,
        in_specs=(P("wave", "space"), P("space", None, None), P("space", None), P("space")),
        out_specs=P("wave", "space"),
        check_vma=False,
    )
```

```python
import jax
import jax.numpy as jnp
from jax import lax
from jax.sharding import PartitionSpec as P

DEGREE = 4
NS_ITERS = 4


def from_behind(shard, axis, by):
    peers = lax.axis_size(axis)
    return lax.ppermute(shard, axis, [(i, (i + by) % peers) for i in range(peers)])


def split_three(values):
    pieces = []
    rest = values
    for piece in range(3):
        head = lax.reduce_precision(rest, exponent_bits=8, mantissa_bits=7)
        pieces.append(head.astype(jnp.bfloat16))
        rest = rest - head
    return jnp.concatenate(pieces, axis=0)


def sum_three(stacked):
    rows = stacked.shape[0] // 3
    return (stacked[:rows] + stacked[rows : 2 * rows]) + stacked[2 * rows :]


def selectors(connectivity, owner_list, node_count):
    plane_count = owner_list.shape[0]
    slots = jnp.arange(node_count + plane_count, dtype=connectivity.dtype)
    pick = (connectivity.reshape(-1)[:, None] == slots[None, :]).astype(jnp.bfloat16)
    owner = (slots[:node_count, None] == owner_list[None, :]).astype(jnp.bfloat16)
    return pick, owner


def apply_filter(wave_block, cell_matrices, pick, owner):
    column_count = wave_block.shape[0]
    node_count = wave_block.shape[1]
    cell_count, cell_nodes, _ = cell_matrices.shape
    own_plane = jnp.dot(wave_block, owner, preferred_element_type=jnp.float32).astype(jnp.bfloat16)
    upper_plane = from_behind(own_plane, "space", -1)
    contract_nodes = (((1,), (1,)), ((), ()))
    gathered = lax.dot_general(
        wave_block, pick[:, :node_count], contract_nodes, preferred_element_type=jnp.float32
    ) + lax.dot_general(
        upper_plane, pick[:, node_count:], contract_nodes, preferred_element_type=jnp.float32
    )
    gathered = gathered.astype(jnp.bfloat16).reshape(column_count, cell_count, cell_nodes)
    products = jnp.einsum(
        "bcn,cnm->bcm", gathered, cell_matrices, preferred_element_type=jnp.float32
    )
    stacked = split_three(products.reshape(column_count, cell_count * cell_nodes))
    plane_part = sum_three(
        jnp.dot(stacked, pick[:, node_count:], preferred_element_type=jnp.float32)
    )
    returned = from_behind(plane_part, "space", 1)
    local_part = sum_three(
        jnp.dot(stacked, pick[:, :node_count], preferred_element_type=jnp.float32)
    )
    back = sum_three(
        lax.dot_general(split_three(returned), owner, contract_nodes, preferred_element_type=jnp.float32)
    )
    return local_part + back


def ring_partners(count):
    steps = []
    stride = 1
    while stride * 2 < count:
        steps.append([position ^ stride for position in range(count)])
        stride *= 2
    quarter = count // 4
    if count >= 4:
        steps.append(
            [
                (position + quarter) % count if (position // quarter) % 2 else (position - quarter) % count
                for position in range(count)
            ]
        )
    elif count == 2:
        steps.append([1, 0])
    return steps


def butterfly_sum(block, axis, inner):
    peers = lax.axis_size(axis)
    outer = peers // inner
    for step in ring_partners(inner):
        pairs = [(i, (i // inner) * inner + step[i % inner]) for i in range(peers)]
        block = block + lax.ppermute(block, axis, pairs)
    for step in ring_partners(outer):
        pairs = [(i, step[i // inner] * inner + i % inner) for i in range(peers)]
        block = block + lax.ppermute(block, axis, pairs)
    return block


def newton_schulz(margin, first_column, width):
    highest = lax.Precision.HIGHEST
    size_cols = margin.shape[0]
    scale = jnp.sqrt(jnp.sum(margin * margin) + 1e-06)
    approx = margin / scale
    identity = jnp.eye(size_cols, dtype=jnp.float32)
    middle = 1.5 * identity - 0.5 * approx
    approx = jnp.dot(approx, middle, precision=highest, preferred_element_type=jnp.float32)
    inverse = middle
    for iteration in range(NS_ITERS - 1):
        middle = 1.5 * identity - 0.5 * jnp.dot(
            inverse, approx, precision=highest, preferred_element_type=jnp.float32
        )
        if iteration == NS_ITERS - 2:
            inverse = lax.dynamic_slice_in_dim(inverse, first_column, width, 1)
        approx = jnp.dot(approx, middle, precision=highest, preferred_element_type=jnp.float32)
        inverse = jnp.dot(middle, inverse, precision=highest, preferred_element_type=jnp.float32)
    return (inverse / jnp.sqrt(scale)).astype(jnp.bfloat16)


def body(wavefunctions, filter_cells, connectivity, owner_list):
    pick, owner = selectors(connectivity, owner_list, wavefunctions.shape[1])
    previous = wavefunctions.astype(jnp.float32)
    current = apply_filter(wavefunctions, filter_cells, pick, owner)
    for degree_step in range(DEGREE - 1):
        following = (
            2.0 * apply_filter(current.astype(jnp.bfloat16), filter_cells, pick, owner)
            - previous
        )
        previous, current = (current, following)
    filtered = current.astype(jnp.bfloat16)
    node_total = filtered.shape[1] * lax.axis_size("space")
    column_count = filtered.shape[0]
    every_column = lax.all_gather(filtered, "wave", axis=0, tiled=True)
    own_rows = jnp.dot(filtered, every_column.T, preferred_element_type=jnp.float32)
    own_rows = butterfly_sum(own_rows, "space", 4)
    margin = lax.all_gather(own_rows, "wave", axis=0, tiled=True) / node_total
    own_rotation = newton_schulz(margin, lax.axis_index("wave") * column_count, column_count)
    return jnp.dot(own_rotation.T, every_column, preferred_element_type=jnp.float32).astype(
        jnp.bfloat16
    )


def solution(mesh):
    return jax.shard_map(
        body,
        mesh=mesh,
        in_specs=(P("wave", "space"), P("space", None, None), P("space", None), P("space")),
        out_specs=P("wave", "space"),
        check_vma=False,
    )
```

```python
import jax
import jax.numpy as jnp
from jax import lax
from jax.sharding import PartitionSpec as P

DEGREE = 4
NS_ITERS = 4


def from_behind(shard, axis, by):
    peers = lax.axis_size(axis)
    return lax.ppermute(shard, axis, [(i, (i + by) % peers) for i in range(peers)])


def split_three(values):
    pieces = []
    rest = values
    for piece in range(3):
        head = lax.reduce_precision(rest, exponent_bits=8, mantissa_bits=7)
        pieces.append(head.astype(jnp.bfloat16))
        rest = rest - head
    return jnp.concatenate(pieces, axis=0)


def sum_three(stacked):
    rows = stacked.shape[0] // 3
    return (stacked[:rows] + stacked[rows : 2 * rows]) + stacked[2 * rows :]


def selectors(connectivity, owner_list, node_count):
    plane_count = owner_list.shape[0]
    slots = jnp.arange(node_count + plane_count, dtype=connectivity.dtype)
    pick = (connectivity.reshape(-1)[:, None] == slots[None, :]).astype(jnp.bfloat16)
    owner = (slots[:node_count, None] == owner_list[None, :]).astype(jnp.bfloat16)
    return pick, owner


def apply_filter(wave_block, cell_matrices, pick, owner, own_plane=None):
    column_count = wave_block.shape[0]
    node_count = wave_block.shape[1]
    cell_count, cell_nodes, _ = cell_matrices.shape
    if own_plane is None:
        own_plane = jnp.dot(wave_block, owner, preferred_element_type=jnp.float32).astype(jnp.bfloat16)
    upper_plane = from_behind(own_plane, "space", -1)
    contract_nodes = (((1,), (1,)), ((), ()))
    gathered = lax.dot_general(
        wave_block, pick[:, :node_count], contract_nodes, preferred_element_type=jnp.float32
    ) + lax.dot_general(
        upper_plane, pick[:, node_count:], contract_nodes, preferred_element_type=jnp.float32
    )
    gathered = gathered.astype(jnp.bfloat16).reshape(column_count, cell_count, cell_nodes)
    products = jnp.einsum(
        "bcn,cnm->bcm", gathered, cell_matrices, preferred_element_type=jnp.float32
    )
    stacked = split_three(products.reshape(column_count, cell_count * cell_nodes))
    plane_part = sum_three(
        jnp.dot(stacked, pick[:, node_count:], preferred_element_type=jnp.float32)
    )
    returned = from_behind(plane_part, "space", 1)
    local_part = sum_three(
        jnp.dot(stacked, pick[:, :node_count], preferred_element_type=jnp.float32)
    )
    back = sum_three(
        lax.dot_general(split_three(returned), owner, contract_nodes, preferred_element_type=jnp.float32)
    )
    return local_part + back


def ring_partners(count):
    steps = []
    stride = 1
    while stride * 2 < count:
        steps.append([position ^ stride for position in range(count)])
        stride *= 2
    quarter = count // 4
    if count >= 4:
        steps.append(
            [
                (position + quarter) % count if (position // quarter) % 2 else (position - quarter) % count
                for position in range(count)
            ]
        )
    elif count == 2:
        steps.append([1, 0])
    return steps


def butterfly_sum(block, axis, inner):
    peers = lax.axis_size(axis)
    outer = peers // inner
    for step in ring_partners(inner):
        pairs = [(i, (i // inner) * inner + step[i % inner]) for i in range(peers)]
        block = block + lax.ppermute(block, axis, pairs)
    for step in ring_partners(outer):
        pairs = [(i, step[i // inner] * inner + i % inner) for i in range(peers)]
        block = block + lax.ppermute(block, axis, pairs)
    return block


def newton_schulz(margin, first_column, width):
    highest = lax.Precision.HIGHEST
    size_cols = margin.shape[0]
    scale = jnp.sqrt(jnp.sum(margin * margin) + 1e-06)
    approx = margin / scale
    identity = jnp.eye(size_cols, dtype=jnp.float32)
    middle = 1.5 * identity - 0.5 * approx
    approx = jnp.dot(approx, middle, precision=highest, preferred_element_type=jnp.float32)
    inverse = middle
    for iteration in range(NS_ITERS - 1):
        middle = 1.5 * identity - 0.5 * jnp.dot(
            inverse, approx, precision=highest, preferred_element_type=jnp.float32
        )
        if iteration == NS_ITERS - 2:
            inverse = lax.dynamic_slice_in_dim(inverse, first_column, width, 1)
        approx = jnp.dot(approx, middle, precision=highest, preferred_element_type=jnp.float32)
        inverse = jnp.dot(middle, inverse, precision=highest, preferred_element_type=jnp.float32)
    return (inverse / jnp.sqrt(scale)).astype(jnp.bfloat16)


def body(wavefunctions, filter_cells, connectivity, owner_list):
    pick, owner = selectors(connectivity, owner_list, wavefunctions.shape[1])
    previous = wavefunctions.astype(jnp.float32)
    current = apply_filter(
        wavefunctions, filter_cells, pick, owner, jnp.take(wavefunctions, owner_list, axis=1)
    )
    for degree_step in range(DEGREE - 1):
        following = (
            2.0 * apply_filter(current.astype(jnp.bfloat16), filter_cells, pick, owner)
            - previous
        )
        previous, current = (current, following)
    filtered = current.astype(jnp.bfloat16)
    node_total = filtered.shape[1] * lax.axis_size("space")
    column_count = filtered.shape[0]
    every_column = lax.all_gather(filtered, "wave", axis=0, tiled=True)
    own_rows = jnp.dot(filtered, every_column.T, preferred_element_type=jnp.float32)
    own_rows = butterfly_sum(own_rows, "space", 4)
    margin = lax.all_gather(own_rows, "wave", axis=0, tiled=True) / node_total
    own_rotation = newton_schulz(margin, lax.axis_index("wave") * column_count, column_count)
    return jnp.dot(own_rotation.T, every_column, preferred_element_type=jnp.float32).astype(
        jnp.bfloat16
    )


def solution(mesh):
    return jax.shard_map(
        body,
        mesh=mesh,
        in_specs=(P("wave", "space"), P("space", None, None), P("space", None), P("space")),
        out_specs=P("wave", "space"),
        check_vma=False,
    )
```

```python
import jax
import jax.numpy as jnp
from jax import lax
from jax.sharding import PartitionSpec as P

DEGREE = 4
NS_ITERS = 4


def from_behind(shard, axis, by):
    peers = lax.axis_size(axis)
    return lax.ppermute(shard, axis, [(i, (i + by) % peers) for i in range(peers)])


def split_three(values):
    pieces = []
    rest = values
    for piece in range(3):
        head = lax.reduce_precision(rest, exponent_bits=8, mantissa_bits=7)
        pieces.append(head.astype(jnp.bfloat16))
        rest = rest - head
    return jnp.concatenate(pieces, axis=0)


def sum_three(stacked):
    rows = stacked.shape[0] // 3
    return (stacked[:rows] + stacked[rows : 2 * rows]) + stacked[2 * rows :]


def selectors(connectivity, owner_list, node_count):
    plane_count = owner_list.shape[0]
    slots = jnp.arange(node_count + plane_count, dtype=connectivity.dtype)
    pick = (connectivity.reshape(-1)[:, None] == slots[None, :]).astype(jnp.bfloat16)
    owner = (slots[:node_count, None] == owner_list[None, :]).astype(jnp.bfloat16)
    return pick, owner


def apply_filter(wave_block, cell_matrices, pick, owner):
    column_count = wave_block.shape[0]
    node_count = wave_block.shape[1]
    cell_count, cell_nodes, _ = cell_matrices.shape
    own_plane = jnp.dot(wave_block, owner, preferred_element_type=jnp.float32).astype(jnp.bfloat16)
    upper_plane = from_behind(own_plane, "space", -1)
    contract_nodes = (((1,), (1,)), ((), ()))
    gathered = lax.dot_general(
        wave_block, pick[:, :node_count], contract_nodes, preferred_element_type=jnp.float32
    ) + lax.dot_general(
        upper_plane, pick[:, node_count:], contract_nodes, preferred_element_type=jnp.float32
    )
    gathered = gathered.astype(jnp.bfloat16).reshape(column_count, cell_count, cell_nodes)
    products = jnp.einsum(
        "bcn,cnm->bcm", gathered, cell_matrices, preferred_element_type=jnp.float32
    )
    stacked = split_three(products.reshape(column_count, cell_count * cell_nodes))
    plane_part = sum_three(
        jnp.dot(stacked, pick[:, node_count:], preferred_element_type=jnp.float32)
    )
    returned = from_behind(plane_part, "space", 1)
    local_part = sum_three(
        jnp.dot(stacked, pick[:, :node_count], preferred_element_type=jnp.float32)
    )
    back = sum_three(
        lax.dot_general(split_three(returned), owner, contract_nodes, preferred_element_type=jnp.float32)
    )
    return local_part + back


def ring_partners(count):
    steps = []
    stride = 1
    while stride * 2 < count:
        steps.append([position ^ stride for position in range(count)])
        stride *= 2
    quarter = count // 4
    if count >= 4:
        steps.append(
            [
                (position + quarter) % count if (position // quarter) % 2 else (position - quarter) % count
                for position in range(count)
            ]
        )
    elif count == 2:
        steps.append([1, 0])
    return steps


def butterfly_sum(block, axis, inner):
    peers = lax.axis_size(axis)
    outer = peers // inner
    for step in ring_partners(inner):
        pairs = [(i, (i // inner) * inner + step[i % inner]) for i in range(peers)]
        block = block + lax.ppermute(block, axis, pairs)
    for step in ring_partners(outer):
        pairs = [(i, step[i // inner] * inner + i % inner) for i in range(peers)]
        block = block + lax.ppermute(block, axis, pairs)
    return block


def newton_schulz(margin, first_column, width):
    highest = lax.Precision.HIGHEST
    size_cols = margin.shape[0]
    scale = jnp.sqrt(jnp.sum(margin * margin) + 1e-06)
    approx = margin / scale
    identity = jnp.eye(size_cols, dtype=jnp.float32)
    middle = 1.5 * identity - 0.5 * approx
    approx = jnp.dot(approx, middle, precision=highest, preferred_element_type=jnp.float32)
    inverse = middle
    for iteration in range(NS_ITERS - 1):
        middle = 1.5 * identity - 0.5 * jnp.dot(
            inverse, approx, precision=highest, preferred_element_type=jnp.float32
        )
        if iteration == NS_ITERS - 2:
            inverse = lax.dynamic_slice_in_dim(inverse, first_column, width, 1)
        approx = jnp.dot(approx, middle, precision=highest, preferred_element_type=jnp.float32)
        inverse = jnp.dot(middle, inverse, precision=highest, preferred_element_type=jnp.float32)
    return (inverse / jnp.sqrt(scale)).astype(jnp.bfloat16)


def body(wavefunctions, filter_cells, connectivity, owner_list):
    pick, owner = selectors(connectivity, owner_list, wavefunctions.shape[1])
    previous = wavefunctions.astype(jnp.float32)
    current = apply_filter(wavefunctions, filter_cells, pick, owner)
    for degree_step in range(DEGREE - 1):
        following = (
            2.0 * apply_filter(current.astype(jnp.bfloat16), filter_cells, pick, owner)
            - previous
        )
        previous, current = (current, following)
    filtered = current.astype(jnp.bfloat16)
    node_total = filtered.shape[1] * lax.axis_size("space")
    column_count = filtered.shape[0]
    every_column = lax.all_gather(filtered, "wave", axis=0, tiled=True)
    own_rows = jnp.dot(filtered, every_column.T, preferred_element_type=jnp.float32)
    own_rows = butterfly_sum(own_rows, "space", 4)
    margin = lax.all_gather(own_rows / node_total, "wave", axis=0, tiled=True)
    own_rotation = newton_schulz(margin, lax.axis_index("wave") * column_count, column_count)
    return jnp.dot(own_rotation.T, every_column, preferred_element_type=jnp.float32).astype(
        jnp.bfloat16
    )


def solution(mesh):
    return jax.shard_map(
        body,
        mesh=mesh,
        in_specs=(P("wave", "space"), P("space", None, None), P("space", None), P("space")),
        out_specs=P("wave", "space"),
        check_vma=False,
    )
```
